256 devices in a mesh: expert: 16 (over z, core), fsdp: 16 (over x, y).
Axes of the slice: x: 4, y: 4, z: 8, core: 2. Of those that a mesh axis runs over, the one named last changes fastest.
Arguments:
- tokens: bfloat16 [4096, 6144], P(('expert', 'fsdp')), may hold values from -6 to 6
- expert_ids: int32 [4096, 4], P(('expert', 'fsdp')), may hold values from 0 to 15, all different within a row; in each aligned block of 16 rows (0 to 15, 16 to 31, ...) at most 5 rows name the same one
- router_weight: float32 [4096, 4], P(('expert', 'fsdp')), may hold values from 0.1 to 1
- w_gate: bfloat16 [16, 5376, 6144], P('expert', 'fsdp'), may hold values from -0.078125 to 0.078125
- w_up: bfloat16 [16, 5376, 6144], P('expert', 'fsdp'), may hold values from -0.078125 to 0.078125
Outputs:
- routed: bfloat16 [4096, 4, 5376], P(('expert', 'fsdp'))
The draws below stay inside these ranges and needn't reach their ends.
Inputs may be any that keep to these rules, and one draw needn't show every extreme that they name: `expert_ids`: each row names 4 different experts; the 16 rows of one device name any one expert at most 5 times, and some device names some expert exactly 5 times.
All inputs are finite; a program needn't handle non-finite values.
Results may differ from the reference program's by a relative error of at most 0.0049.
Values may be sent and summed in bfloat16 or wider, within the bound.
No kernel may reach another device: no remote copies, remote signals or barrier semaphores. Data moves between devices by JAX's collectives and lax.ppermute only.
A program may use at most 128 MiB of HBM per device.

```python
import math
import jax
import jax.numpy as jnp
import numpy as np
from jax import lax

D = 6144
TOPK = 4
H = 5376
TOK_DEV = 16
EXPERTS = 16
TOKENS = 4096
CAP = 5
GROUP_SLOTS = 1280


def block_levels(own_key, dims, shards, smallest, high):
    gain, own = 1.0, jax.random.fold_in(own_key, 6)
    for axis_at, blocks in shards:
        steps = jnp.exp(jax.random.uniform(jax.random.fold_in(own, axis_at), (blocks,), jnp.float32, smallest / len(shards), high / len(shards)))
        gain = gain * jnp.repeat(steps, dims[axis_at] // blocks).reshape([-1 if axis == axis_at else 1 for axis in range(len(dims))])
    return gain


def assign_block(key, own, number, rows, number_of, top, most, lean):
    order = jax.random.permutation(key, number_of)
    packed, ordinary = shares(number_of, rows * top, most, lean, True), shares(number_of, rows * top, most, lean, False)
    places = jnp.arange(number_of)

    def named(sizes, turn):
        used = int((sizes > 0).sum())
        fixed = max(1, used // 4)
        shifted = fixed + (places - fixed + turn * (used - fixed)) % max(1, number_of - fixed)
        return jnp.zeros((number_of,), jnp.int32).at[order[jnp.where(places < fixed, places, shifted)]].set(jnp.asarray(sizes, jnp.int32))

    sizes = jnp.where(number % 4 == 0, named(packed, number // 4), named(ordinary, number - number // 4 - 1))
    mixed = jax.random.permutation(jax.random.fold_in(own, 3), number_of)
    donor, receiver = mixed[0:number_of // 2 * 2:2], mixed[1:number_of // 2 * 2:2]
    margin = jnp.minimum(sizes[donor] - 1, most - sizes[receiver]) // 2
    margin = jnp.where((donor == order[0]) | (receiver == order[0]) | (sizes[receiver] == 0), 0, jnp.maximum(margin, 0))
    shifted = jax.random.randint(jax.random.fold_in(own, 4), (number_of // 2,), 0, 1 << 20) % (margin + 1)
    sizes = sizes.at[donor].add(-shifted).at[receiver].add(shifted)
    members = jnp.searchsorted(jnp.cumsum(sizes), jnp.arange(rows * top), side="right").astype(jnp.int32)
    listing = members.reshape(top, rows).T
    listing = listing[jax.random.permutation(jax.random.fold_in(own, 1), rows)]
    turn = jax.random.randint(jax.random.fold_in(own, 2), (rows, 1), 0, top)
    return jnp.take_along_axis(listing, (jnp.arange(top)[None, :] + turn) % top, axis=1)


def shares(number_of, total, most, slope, full):
    portions = [(1 << 20) // math.isqrt(grade ** slope) + 1 for grade in range(1, number_of + 1)]
    largest = most if full else min(most, max(-(-total // number_of), total * portions[0] // sum(portions)))
    least = 1 if total - largest >= number_of - 1 else 0
    holding, rest = [largest] + [least] * (number_of - 1), total - largest - least * (number_of - 1)
    while rest > 0:
        free = [i for i in range(1, number_of) if holding[i] < largest] or [i for i in range(1, number_of) if holding[i] < most]
        mass, left = sum([portions[i] for i in free]), rest
        for i in free:
            extra = min(most - holding[i], max(1, left * portions[i] // mass), rest)
            holding[i] = holding[i] + extra
            rest = rest - extra
    return np.array(holding)


def scatter_about(stream_key, extent, width, limit, split=(), kind=jnp.bfloat16):
    entries = jax.random.normal(stream_key, extent, jnp.float32) * width
    if len(split) > 0:
        entries = block_levels(stream_key, extent, split, -0.22, 0.18) * entries
    return jnp.clip(entries, min=-limit, max=limit).astype(kind)


def setup_inputs(seed: int = 0) -> dict:
    key_of = jax.random.split(jax.random.key(seed), 6)
    tokens = scatter_about(key_of[0], (TOKENS, D), 1.0, 6.0, ((0, 256),))
    expert_ids_keys = jax.random.split(jax.random.fold_in(key_of[1], 1), TOKENS // TOK_DEV)
    expert_ids_turns = jax.random.permutation(jax.random.fold_in(key_of[1], 3), TOKENS // TOK_DEV)
    expert_ids = jax.vmap(lambda own, number: assign_block(jax.random.fold_in(key_of[1], 2), own, number, TOK_DEV, EXPERTS, TOPK, CAP, 2))(expert_ids_keys, expert_ids_turns).reshape((TOKENS, TOPK))
    router_weight = jnp.clip(0.1 + 0.9 * jax.random.uniform(key_of[2], (TOKENS, TOPK), jnp.float32) ** block_levels(key_of[2], (TOKENS, TOPK), ((0, 256),), -0.2, 0.2), 0.1, 1.0)
    w_gate = scatter_about(key_of[3], (EXPERTS, H, D), D ** -0.5, 0.078125, ((0, 16), (1, 16)))
    w_up = scatter_about(key_of[4], (EXPERTS, H, D), D ** -0.5, 0.078125, ((0, 16), (1, 16)))
    return dict(tokens=tokens, expert_ids=expert_ids, router_weight=router_weight, w_gate=w_gate, w_up=w_up)


def reference(tokens, expert_ids, router_weight, w_gate, w_up):
    flat_ids = expert_ids.reshape(-1).astype(jnp.int32)
    rows_all = TOKENS * TOPK

    def one_expert(hidden_all, expert):
        picked = jnp.nonzero(flat_ids == expert, size=GROUP_SLOTS, fill_value=rows_all)[0].astype(jnp.int32)
        token_index = jnp.minimum(picked // TOPK, TOKENS - 1).astype(jnp.int32)
        token_rows = jnp.take(tokens, token_index, axis=0)
        gate_rows = lax.dynamic_index_in_dim(w_gate, expert, 0, keepdims=False)
        up_rows = lax.dynamic_index_in_dim(w_up, expert, 0, keepdims=False)
        gate_act = jnp.dot(token_rows, gate_rows.T, preferred_element_type=jnp.float32)
        up_act = jnp.dot(token_rows, up_rows.T, preferred_element_type=jnp.float32)
        hidden = (jax.nn.gelu(gate_act, approximate=False) * up_act).astype(jnp.bfloat16)
        return hidden_all.at[picked].set(hidden, mode="drop"), None

    start_value = jnp.zeros((rows_all, H), jnp.bfloat16)
    hidden_all = lax.scan(one_expert, start_value, jnp.arange(EXPERTS, dtype=jnp.int32))[0]
    routed = (router_weight.reshape(-1, 1) * hidden_all.astype(jnp.float32)).astype(jnp.bfloat16)
    return routed.reshape(TOKENS, TOPK, H)
```

```python
import jax
import jax.numpy as jnp
from jax import lax
from jax.sharding import PartitionSpec as P


def hidden_block(row_block, gate_rows, up_rows):
    gate_act = lax.dot_general(
        row_block, gate_rows, (((1,), (1,)), ((), ())), preferred_element_type=jnp.float32
    )
    up_act = lax.dot_general(
        row_block, up_rows, (((1,), (1,)), ((), ())), preferred_element_type=jnp.float32
    )
    return (jax.nn.gelu(gate_act, approximate=False) * up_act).astype(jnp.bfloat16)


def local(tokens, expert_ids, router_weight, w_gate, w_up):
    tok_rows, model_width = tokens.shape
    top_count = expert_ids.shape[1]
    experts = lax.axis_size("expert")
    fsdp_size = lax.axis_size("fsdp")
    cap_slots = 5 * tok_rows * top_count // (4 * experts)
    flat_ids = expert_ids.reshape(-1)
    choosing = (flat_ids[:, None] == jnp.arange(experts, dtype=jnp.int32)[None, :]).astype(
        jnp.int32
    )
    slot_rank = jnp.sum((jnp.cumsum(choosing, axis=0) - 1) * choosing, axis=1)
    slot_of = flat_ids * cap_slots + slot_rank
    placing = (
        slot_of[None, :] == jnp.arange(experts * cap_slots, dtype=jnp.int32)[:, None]
    ).astype(jnp.bfloat16)
    repeated = jnp.repeat(tokens, top_count, axis=0)
    outgoing = jnp.dot(placing, repeated, preferred_element_type=jnp.float32).astype(jnp.bfloat16)
    outgoing = outgoing.reshape(experts, cap_slots, model_width)
    gate_rows = w_gate[0]
    up_rows = w_up[0]
    columns = gate_rows.shape[0]
    arrived = lax.all_to_all(outgoing, "expert", split_axis=0, concat_axis=0, tiled=True)
    local_hidden = hidden_block(
        lax.all_gather(arrived.reshape(-1, model_width), "fsdp", axis=0, tiled=True),
        gate_rows,
        up_rows,
    )
    shaped = local_hidden.reshape(fsdp_size, experts, cap_slots, columns)
    by_owner = jnp.transpose(shaped, (1, 0, 2, 3)).reshape(experts * fsdp_size, cap_slots, columns)
    returned = lax.all_to_all(by_owner, ("expert", "fsdp"), 0, 0, tiled=True)
    returned = returned.reshape(experts, fsdp_size, cap_slots, columns)
    returned = jnp.transpose(returned, (0, 2, 1, 3)).reshape(experts * cap_slots, -1)
    collected = lax.dot_general(
        placing, returned, (((0,), (0,)), ((), ())), preferred_element_type=jnp.float32
    )
    routed = (router_weight.reshape(-1, 1) * collected).astype(jnp.bfloat16)
    return routed.reshape(tok_rows, top_count, -1)


def solution(mesh):
    return jax.shard_map(
        local,
        mesh=mesh,
        in_specs=(
            P(("expert", "fsdp"), None),
            P(("expert", "fsdp"), None),
            P(("expert", "fsdp"), None),
            P("expert", "fsdp", None),
            P("expert", "fsdp", None),
        ),
        out_specs=P(("expert", "fsdp"), None, None),
        check_vma=False,
    )
```

```python
import jax
import jax.numpy as jnp
from jax import lax
from jax.sharding import PartitionSpec as P


def hidden_block(row_block, gate_rows, up_rows):
    gate_act = lax.dot_general(
        row_block, gate_rows, (((1,), (1,)), ((), ())), preferred_element_type=jnp.float32
    )
    up_act = lax.dot_general(
        row_block, up_rows, (((1,), (1,)), ((), ())), preferred_element_type=jnp.float32
    )
    return (jax.nn.gelu(gate_act, approximate=False) * up_act).astype(jnp.bfloat16)


def local(tokens, expert_ids, router_weight, w_gate, w_up):
    tok_rows, model_width = tokens.shape
    top_count = expert_ids.shape[1]
    experts = lax.axis_size("expert")
    fsdp_size = lax.axis_size("fsdp")
    cap_slots = 5 * tok_rows * top_count // (4 * experts)
    flat_ids = expert_ids.reshape(-1)
    choosing = (flat_ids[:, None] == jnp.arange(experts, dtype=jnp.int32)[None, :]).astype(
        jnp.int32
    )
    slot_rank = jnp.sum((jnp.cumsum(choosing, axis=0) - 1) * choosing, axis=1)
    slot_of = flat_ids * cap_slots + slot_rank
    placing = (
        slot_of[None, :] == jnp.arange(experts * cap_slots, dtype=jnp.int32)[:, None]
    ).astype(jnp.bfloat16)
    repeated = jnp.repeat(tokens, top_count, axis=0)
    outgoing = jnp.dot(placing, repeated, preferred_element_type=jnp.float32).astype(jnp.bfloat16)
    outgoing = outgoing.reshape(experts, cap_slots, model_width)
    gate_rows = w_gate[0]
    up_rows = w_up[0]
    columns = gate_rows.shape[0]
    block = cap_slots * model_width
    dense = outgoing.reshape(experts, block // 128, 128)
    arrived = lax.all_to_all(dense, "expert", split_axis=0, concat_axis=0, tiled=True)
    local_hidden = hidden_block(
        lax.all_gather(arrived.reshape(-1, model_width), "fsdp", axis=0, tiled=True),
        gate_rows,
        up_rows,
    )
    shaped = local_hidden.reshape(fsdp_size, experts, cap_slots, columns)
    by_owner = jnp.transpose(shaped, (1, 0, 2, 3)).reshape(experts * fsdp_size, 16, -1)
    returned = lax.all_to_all(by_owner, ("expert", "fsdp"), 0, 0, tiled=True)
    returned = returned.reshape(experts, fsdp_size, cap_slots, columns)
    returned = jnp.transpose(returned, (0, 2, 1, 3)).reshape(experts * cap_slots, -1)
    collected = lax.dot_general(
        placing, returned, (((0,), (0,)), ((), ())), preferred_element_type=jnp.float32
    )
    routed = (router_weight.reshape(-1, 1) * collected).astype(jnp.bfloat16)
    return routed.reshape(tok_rows, top_count, -1)


def solution(mesh):
    return jax.shard_map(
        local,
        mesh=mesh,
        in_specs=(
            P(("expert", "fsdp"), None),
            P(("expert", "fsdp"), None),
            P(("expert", "fsdp"), None),
            P("expert", "fsdp", None),
            P("expert", "fsdp", None),
        ),
        out_specs=P(("expert", "fsdp"), None, None),
        check_vma=False,
    )
```

```python
import jax
import jax.numpy as jnp
from jax import lax
from jax.sharding import PartitionSpec as P


def hidden_block(row_block, gate_rows, up_rows):
    columns = gate_rows.shape[0]
    both = jnp.concatenate([gate_rows, up_rows], axis=0)
    acts = lax.dot_general(
        row_block, both, (((1,), (1,)), ((), ())), preferred_element_type=jnp.float32
    )
    gate_act = acts[:, :columns]
    up_act = acts[:, columns:]
    return (jax.nn.gelu(gate_act, approximate=False) * up_act).astype(jnp.bfloat16)


def local(tokens, expert_ids, router_weight, w_gate, w_up):
    tok_rows, model_width = tokens.shape
    top_count = expert_ids.shape[1]
    experts = lax.axis_size("expert")
    fsdp_size = lax.axis_size("fsdp")
    cap_slots = 5 * tok_rows * top_count // (4 * experts)
    flat_ids = expert_ids.reshape(-1)
    choosing = (flat_ids[:, None] == jnp.arange(experts, dtype=jnp.int32)[None, :]).astype(
        jnp.int32
    )
    slot_rank = jnp.sum((jnp.cumsum(choosing, axis=0) - 1) * choosing, axis=1)
    slot_of = flat_ids * cap_slots + slot_rank
    placing = (
        slot_of[None, :] == jnp.arange(experts * cap_slots, dtype=jnp.int32)[:, None]
    ).astype(jnp.bfloat16)
    repeated = jnp.repeat(tokens, top_count, axis=0)
    outgoing = jnp.dot(placing, repeated, preferred_element_type=jnp.float32).astype(jnp.bfloat16)
    outgoing = outgoing.reshape(experts, cap_slots, model_width)
    gate_rows = w_gate[0]
    up_rows = w_up[0]
    columns = gate_rows.shape[0]
    block = cap_slots * model_width
    dense = outgoing.reshape(experts, block // 128, 128)
    arrived = lax.all_to_all(dense, "expert", split_axis=0, concat_axis=0, tiled=True)
    local_hidden = hidden_block(
        lax.all_gather(arrived.reshape(-1, model_width), "fsdp", axis=0, tiled=True),
        gate_rows,
        up_rows,
    )
    shaped = local_hidden.reshape(fsdp_size, experts, cap_slots, columns)
    by_owner = jnp.transpose(shaped, (1, 0, 2, 3)).reshape(experts * fsdp_size, 16, -1)
    returned = lax.all_to_all(by_owner, ("expert", "fsdp"), 0, 0, tiled=True)
    returned = returned.reshape(experts, fsdp_size, cap_slots, columns)
    returned = jnp.transpose(returned, (0, 2, 1, 3)).reshape(experts * cap_slots, -1)
    collected = lax.dot_general(
        placing, returned, (((0,), (0,)), ((), ())), preferred_element_type=jnp.float32
    )
    routed = (router_weight.reshape(-1, 1) * collected).astype(jnp.bfloat16)
    return routed.reshape(tok_rows, top_count, -1)


def solution(mesh):
    return jax.shard_map(
        local,
        mesh=mesh,
        in_specs=(
            P(("expert", "fsdp"), None),
            P(("expert", "fsdp"), None),
            P(("expert", "fsdp"), None),
            P("expert", "fsdp", None),
            P("expert", "fsdp", None),
        ),
        out_specs=P(("expert", "fsdp"), None, None),
        check_vma=False,
    )
```

```python
import jax
import jax.numpy as jnp
from jax import lax
from jax.sharding import PartitionSpec as P


def hidden_block(row_block, gate_rows, up_rows):
    columns = gate_rows.shape[0]
    both = jnp.concatenate([gate_rows, up_rows], axis=0)
    acts = lax.dot_general(
        row_block, both, (((1,), (1,)), ((), ())), preferred_element_type=jnp.float32
    )
    gate_act = acts[:, :columns]
    up_act = acts[:, columns:]
    return (jax.nn.gelu(gate_act, approximate=False) * up_act).astype(jnp.bfloat16)


def local(tokens, expert_ids, router_weight, w_gate, w_up):
    tok_rows, model_width = tokens.shape
    top_count = expert_ids.shape[1]
    experts = lax.axis_size("expert")
    fsdp_size = lax.axis_size("fsdp")
    cap_slots = 5 * tok_rows * top_count // (4 * experts)
    flat_ids = expert_ids.reshape(-1)
    choosing = (flat_ids[:, None] == jnp.arange(experts, dtype=jnp.int32)[None, :]).astype(
        jnp.int32
    )
    slot_rank = jnp.sum((jnp.cumsum(choosing, axis=0) - 1) * choosing, axis=1)
    slot_of = flat_ids * cap_slots + slot_rank
    slots = jnp.arange(experts * cap_slots, dtype=jnp.int32)
    placing = (slot_of.reshape(tok_rows, top_count)[:, :, None] == slots).astype(jnp.bfloat16)
    by_token = jnp.sum(placing, axis=1)
    outgoing = lax.dot_general(
        by_token, tokens, (((0,), (0,)), ((), ())), preferred_element_type=jnp.float32
    ).astype(jnp.bfloat16)
    outgoing = outgoing.reshape(experts, cap_slots, model_width)
    gate_rows = w_gate[0]
    up_rows = w_up[0]
    columns = gate_rows.shape[0]
    block = cap_slots * model_width
    dense = outgoing.reshape(experts, block // 128, 128)
    arrived = lax.all_to_all(dense, "expert", split_axis=0, concat_axis=0, tiled=True)
    local_hidden = hidden_block(
        lax.all_gather(arrived.reshape(-1, model_width), "fsdp", axis=0, tiled=True),
        gate_rows,
        up_rows,
    )
    shaped = local_hidden.reshape(fsdp_size, experts, cap_slots, columns)
    by_owner = jnp.transpose(shaped, (1, 0, 2, 3)).reshape(experts * fsdp_size, 16, -1)
    returned = lax.all_to_all(by_owner, ("expert", "fsdp"), 0, 0, tiled=True)
    returned = returned.reshape(experts, fsdp_size, cap_slots, columns)
    returned = jnp.transpose(returned, (0, 2, 1, 3)).reshape(experts * cap_slots, -1)
    collected = lax.dot_general(
        placing, returned, (((2,), (0,)), ((), ())), preferred_element_type=jnp.float32
    )
    return (router_weight[:, :, None] * collected).astype(jnp.bfloat16)


def solution(mesh):
    return jax.shard_map(
        local,
        mesh=mesh,
        in_specs=(
            P(("expert", "fsdp"), None),
            P(("expert", "fsdp"), None),
            P(("expert", "fsdp"), None),
            P("expert", "fsdp", None),
            P("expert", "fsdp", None),
        ),
        out_specs=P(("expert", "fsdp"), None, None),
        check_vma=False,
    )
```

```python
import jax
import jax.numpy as jnp
from jax import lax
from jax.sharding import PartitionSpec as P


def hidden_block(row_block, gate_rows, up_rows):
    columns = gate_rows.shape[0]
    both = jnp.concatenate([gate_rows, up_rows], axis=0)
    acts = lax.dot_general(
        row_block, both, (((1,), (1,)), ((), ())), preferred_element_type=jnp.float32
    )
    gate_act = acts[:, :columns]
    up_act = acts[:, columns:]
    return (jax.nn.gelu(gate_act, approximate=False) * up_act).astype(jnp.bfloat16)


def local(tokens, expert_ids, router_weight, w_gate, w_up):
    tok_rows, model_width = tokens.shape
    top_count = expert_ids.shape[1]
    experts = lax.axis_size("expert")
    fsdp_size = lax.axis_size("fsdp")
    cap_slots = 5 * tok_rows * top_count // (4 * experts)
    flat_ids = expert_ids.reshape(-1)
    choosing = (flat_ids[:, None] == jnp.arange(experts, dtype=jnp.int32)[None, :]).astype(
        jnp.int32
    )
    slot_rank = jnp.sum((jnp.cumsum(choosing, axis=0) - 1) * choosing, axis=1)
    slot_of = flat_ids * cap_slots + slot_rank
    slots = jnp.arange(experts * cap_slots, dtype=jnp.int32)
    placing = (slot_of.reshape(tok_rows, top_count)[:, :, None] == slots).astype(jnp.bfloat16)
    by_token = jnp.sum(placing, axis=1)
    outgoing = lax.dot_general(
        by_token, tokens, (((0,), (0,)), ((), ())), preferred_element_type=jnp.float32
    ).astype(jnp.bfloat16)
    outgoing = outgoing.reshape(experts, cap_slots, model_width)
    gate_rows = w_gate[0]
    up_rows = w_up[0]
    columns = gate_rows.shape[0]
    block = cap_slots * model_width
    dense = outgoing.reshape(experts, block // 128, 128)
    arrived = lax.all_to_all(dense, "expert", split_axis=0, concat_axis=0, tiled=True)
    local_hidden = hidden_block(
        lax.all_gather(arrived.reshape(-1, model_width), "fsdp", axis=0, tiled=True),
        gate_rows,
        up_rows,
    )
    shaped = local_hidden.reshape(fsdp_size, experts, cap_slots, columns)
    wide = -(-columns // 128) * 128
    by_owner = jnp.transpose(shaped, (1, 0, 2, 3))
    by_owner = jnp.pad(by_owner, ((0, 0), (0, 0), (0, 0), (0, wide - columns)))
    by_owner = by_owner.reshape(experts * fsdp_size, cap_slots * wide // 128, 128)
    returned = lax.all_to_all(by_owner, ("expert", "fsdp"), 0, 0, tiled=True)
    returned = returned.reshape(experts, fsdp_size, cap_slots, wide)[..., :columns]
    returned = jnp.transpose(returned, (0, 2, 1, 3)).reshape(experts * cap_slots, -1)
    collected = lax.dot_general(
        placing, returned, (((2,), (0,)), ((), ())), preferred_element_type=jnp.float32
    )
    return (router_weight[:, :, None] * collected).astype(jnp.bfloat16)


def solution(mesh):
    return jax.shard_map(
        local,
        mesh=mesh,
        in_specs=(
            P(("expert", "fsdp"), None),
            P(("expert", "fsdp"), None),
            P(("expert", "fsdp"), None),
            P("expert", "fsdp", None),
            P("expert", "fsdp", None),
        ),
        out_specs=P(("expert", "fsdp"), None, None),
        check_vma=False,
    )
```

```python
import jax
import jax.numpy as jnp
from jax import lax
from jax.sharding import PartitionSpec as P
from jax.experimental import pallas as pl
from jax.experimental.pallas import tpu as pltpu


def _hidden_kernel(rows_ref, gate_ref, up_ref, out_ref):
    rows = rows_ref[...]
    dims = (((1,), (1,)), ((), ()))
    gate_act = lax.dot_general(rows, gate_ref[...], dims, preferred_element_type=jnp.float32)
    up_act = lax.dot_general(rows, up_ref[...], dims, preferred_element_type=jnp.float32)
    gelu = gate_act * (1.0 + lax.erf(gate_act * (2.0 ** -0.5))) * 0.5
    out_ref[...] = (gelu * up_act).astype(out_ref.dtype)


def hidden_block(row_block, gate_rows, up_rows):
    count, width = row_block.shape
    columns = gate_rows.shape[0]
    tile = 128
    return pl.pallas_call(
        _hidden_kernel,
        grid=(count // tile,),
        in_specs=[
            pl.BlockSpec((tile, width), lambda i: (i, 0)),
            pl.BlockSpec(memory_space=pltpu.VMEM),
            pl.BlockSpec(memory_space=pltpu.VMEM),
        ],
        out_specs=pl.BlockSpec((tile, columns), lambda i: (i, 0)),
        out_shape=jax.ShapeDtypeStruct((count, columns), jnp.bfloat16),
        compiler_params=pltpu.CompilerParams(vmem_limit_bytes=48 * 1024 * 1024),
        cost_estimate=pl.CostEstimate(
            flops=4 * count * width * columns,
            transcendentals=count * columns,
            bytes_accessed=2 * (count * width + 2 * columns * width + count * columns),
        ),
    )(row_block, gate_rows, up_rows)


def local(tokens, expert_ids, router_weight, w_gate, w_up):
    tok_rows, model_width = tokens.shape
    top_count = expert_ids.shape[1]
    experts = lax.axis_size("expert")
    fsdp_size = lax.axis_size("fsdp")
    cap_slots = 5 * tok_rows * top_count // (4 * experts)
    flat_ids = expert_ids.reshape(-1)
    choosing = (flat_ids[:, None] == jnp.arange(experts, dtype=jnp.int32)[None, :]).astype(
        jnp.int32
    )
    slot_rank = jnp.sum((jnp.cumsum(choosing, axis=0) - 1) * choosing, axis=1)
    slot_of = flat_ids * cap_slots + slot_rank
    slots = jnp.arange(experts * cap_slots, dtype=jnp.int32)
    placing = (slot_of.reshape(tok_rows, top_count)[:, :, None] == slots).astype(jnp.bfloat16)
    by_token = jnp.sum(placing, axis=1)
    outgoing = lax.dot_general(
        by_token, tokens, (((0,), (0,)), ((), ())), preferred_element_type=jnp.float32
    ).astype(jnp.bfloat16)
    outgoing = outgoing.reshape(experts, cap_slots, model_width)
    gate_rows = w_gate[0]
    up_rows = w_up[0]
    columns = gate_rows.shape[0]
    block = cap_slots * model_width
    dense = outgoing.reshape(experts, block // 128, 128)
    arrived = lax.all_to_all(dense, "expert", split_axis=0, concat_axis=0, tiled=True)
    local_hidden = hidden_block(
        lax.all_gather(arrived.reshape(-1, model_width), "fsdp", axis=0, tiled=True),
        gate_rows,
        up_rows,
    )
    shaped = local_hidden.reshape(fsdp_size, experts, cap_slots, columns)
    wide = -(-columns // 128) * 128
    by_owner = jnp.transpose(shaped, (1, 0, 2, 3))
    by_owner = jnp.pad(by_owner, ((0, 0), (0, 0), (0, 0), (0, wide - columns)))
    by_owner = by_owner.reshape(experts * fsdp_size, cap_slots * wide // 128, 128)
    returned = lax.all_to_all(by_owner, ("expert", "fsdp"), 0, 0, tiled=True)
    returned = returned.reshape(experts, fsdp_size, cap_slots, wide)[..., :columns]
    returned = jnp.transpose(returned, (0, 2, 1, 3)).reshape(experts * cap_slots, -1)
    collected = lax.dot_general(
        placing, returned, (((2,), (0,)), ((), ())), preferred_element_type=jnp.float32
    )
    return (router_weight[:, :, None] * collected).astype(jnp.bfloat16)


def solution(mesh):
    return jax.shard_map(
        local,
        mesh=mesh,
        in_specs=(
            P(("expert", "fsdp"), None),
            P(("expert", "fsdp"), None),
            P(("expert", "fsdp"), None),
            P("expert", "fsdp", None),
            P("expert", "fsdp", None),
        ),
        out_specs=P(("expert", "fsdp"), None, None),
        check_vma=False,
    )
```

```python
import jax
import jax.numpy as jnp
from jax import lax
from jax.sharding import PartitionSpec as P
from jax.experimental import pallas as pl
from jax.experimental.pallas import tpu as pltpu


def _hidden_kernel(rows_ref, gate_ref, up_ref, out_ref):
    rows = rows_ref[...]
    gate_act = jnp.dot(rows, gate_ref[...], preferred_element_type=jnp.float32)
    up_act = jnp.dot(rows, up_ref[...], preferred_element_type=jnp.float32)
    gelu = gate_act * (1.0 + lax.erf(gate_act * (2.0 ** -0.5))) * 0.5
    out_ref[...] = (gelu * up_act).astype(out_ref.dtype)


def hidden_block(row_block, gate_rows, up_rows):
    count, width = row_block.shape
    columns = gate_rows.shape[0]
    tile = 256
    return pl.pallas_call(
        _hidden_kernel,
        grid=(count // tile,),
        in_specs=[
            pl.BlockSpec((tile, width), lambda i: (i, 0)),
            pl.BlockSpec(memory_space=pltpu.VMEM),
            pl.BlockSpec(memory_space=pltpu.VMEM),
        ],
        out_specs=pl.BlockSpec((tile, columns), lambda i: (i, 0)),
        out_shape=jax.ShapeDtypeStruct((count, columns), jnp.bfloat16),
        compiler_params=pltpu.CompilerParams(vmem_limit_bytes=48 * 1024 * 1024),
        cost_estimate=pl.CostEstimate(
            flops=4 * count * width * columns,
            transcendentals=count * columns,
            bytes_accessed=2 * (count * width + 2 * columns * width + count * columns),
        ),
    )(row_block, gate_rows.T, up_rows.T)


def local(tokens, expert_ids, router_weight, w_gate, w_up):
    tok_rows, model_width = tokens.shape
    top_count = expert_ids.shape[1]
    experts = lax.axis_size("expert")
    fsdp_size = lax.axis_size("fsdp")
    cap_slots = 5 * tok_rows * top_count // (4 * experts)
    flat_ids = expert_ids.reshape(-1)
    choosing = (flat_ids[:, None] == jnp.arange(experts, dtype=jnp.int32)[None, :]).astype(
        jnp.int32
    )
    slot_rank = jnp.sum((jnp.cumsum(choosing, axis=0) - 1) * choosing, axis=1)
    slot_of = flat_ids * cap_slots + slot_rank
    slots = jnp.arange(experts * cap_slots, dtype=jnp.int32)
    placing = (slot_of.reshape(tok_rows, top_count)[:, :, None] == slots).astype(jnp.bfloat16)
    by_token = jnp.sum(placing, axis=1)
    outgoing = lax.dot_general(
        by_token, tokens, (((0,), (0,)), ((), ())), preferred_element_type=jnp.float32
    ).astype(jnp.bfloat16)
    outgoing = outgoing.reshape(experts, cap_slots, model_width)
    gate_rows = w_gate[0]
    up_rows = w_up[0]
    columns = gate_rows.shape[0]
    block = cap_slots * model_width
    dense = outgoing.reshape(experts, block // 128, 128)
    arrived = lax.all_to_all(dense, "expert", split_axis=0, concat_axis=0, tiled=True)
    local_hidden = hidden_block(
        lax.all_gather(arrived.reshape(-1, model_width), "fsdp", axis=0, tiled=True),
        gate_rows,
        up_rows,
    )
    shaped = local_hidden.reshape(fsdp_size, experts, cap_slots, columns)
    wide = -(-columns // 128) * 128
    by_owner = jnp.transpose(shaped, (1, 0, 2, 3))
    by_owner = jnp.pad(by_owner, ((0, 0), (0, 0), (0, 0), (0, wide - columns)))
    by_owner = by_owner.reshape(experts * fsdp_size, cap_slots * wide // 128, 128)
    returned = lax.all_to_all(by_owner, ("expert", "fsdp"), 0, 0, tiled=True)
    returned = returned.reshape(experts, fsdp_size, cap_slots, wide)[..., :columns]
    returned = jnp.transpose(returned, (0, 2, 1, 3)).reshape(experts * cap_slots, -1)
    collected = lax.dot_general(
        placing, returned, (((2,), (0,)), ((), ())), preferred_element_type=jnp.float32
    )
    return (router_weight[:, :, None] * collected).astype(jnp.bfloat16)


def solution(mesh):
    return jax.shard_map(
        local,
        mesh=mesh,
        in_specs=(
            P(("expert", "fsdp"), None),
            P(("expert", "fsdp"), None),
            P(("expert", "fsdp"), None),
            P("expert", "fsdp", None),
            P("expert", "fsdp", None),
        ),
        out_specs=P(("expert", "fsdp"), None, None),
        check_vma=False,
    )
```

```python
import jax
import jax.numpy as jnp
from jax import lax
from jax.sharding import PartitionSpec as P


def hidden_block(row_block, gate_rows, up_rows):
    columns = gate_rows.shape[0]
    both = jnp.concatenate([gate_rows, up_rows], axis=0)
    acts = lax.dot_general(
        row_block, both, (((1,), (1,)), ((), ())), preferred_element_type=jnp.float32
    )
    gate_act = acts[:, :columns]
    up_act = acts[:, columns:]
    return (jax.nn.gelu(gate_act, approximate=False) * up_act).astype(jnp.bfloat16)


def local(tokens, expert_ids, router_weight, w_gate, w_up):
    tok_rows, model_width = tokens.shape
    top_count = expert_ids.shape[1]
    experts = lax.axis_size("expert")
    fsdp_size = lax.axis_size("fsdp")
    cap_slots = 5 * tok_rows * top_count // (4 * experts)
    flat_ids = expert_ids.reshape(-1)
    choosing = (flat_ids[:, None] == jnp.arange(experts, dtype=jnp.int32)[None, :]).astype(
        jnp.int32
    )
    slot_rank = jnp.sum((jnp.cumsum(choosing, axis=0) - 1) * choosing, axis=1)
    slot_of = flat_ids * cap_slots + slot_rank
    slots = jnp.arange(experts * cap_slots, dtype=jnp.int32)
    placing = (slot_of.reshape(tok_rows, top_count)[:, :, None] == slots).astype(jnp.bfloat16)
    by_token = jnp.sum(placing, axis=1)
    outgoing = lax.dot_general(
        by_token, tokens, (((0,), (0,)), ((), ())), preferred_element_type=jnp.float32
    ).astype(jnp.bfloat16)
    outgoing = outgoing.reshape(experts, cap_slots, model_width)
    gate_rows = w_gate[0]
    up_rows = w_up[0]
    columns = gate_rows.shape[0]
    block = cap_slots * model_width
    dense = outgoing.reshape(experts, block // 128, 128)
    arrived = lax.all_to_all(dense, "expert", split_axis=0, concat_axis=0, tiled=True)
    local_hidden = hidden_block(
        lax.all_gather(arrived.reshape(-1, model_width), "fsdp", axis=0, tiled=True),
        gate_rows,
        up_rows,
    )
    shaped = local_hidden.reshape(fsdp_size, experts, cap_slots, columns)
    wide = -(-columns // 128) * 128
    by_owner = jnp.transpose(shaped, (1, 0, 2, 3))
    by_owner = jnp.pad(by_owner, ((0, 0), (0, 0), (0, 0), (0, wide - columns)))
    by_owner = by_owner.reshape(experts * fsdp_size, cap_slots * wide // 128, 128)
    returned = lax.all_to_all(by_owner, ("expert", "fsdp"), 0, 0, tiled=True)
    returned = returned.reshape(experts, fsdp_size, cap_slots, wide)[..., :columns]
    returned = jnp.transpose(returned, (0, 2, 1, 3)).reshape(experts * cap_slots, -1)
    collected = jnp.take(returned, slot_of.reshape(tok_rows, top_count), axis=0, mode="clip")
    return (router_weight[:, :, None] * collected.astype(jnp.float32)).astype(jnp.bfloat16)


def solution(mesh):
    return jax.shard_map(
        local,
        mesh=mesh,
        in_specs=(
            P(("expert", "fsdp"), None),
            P(("expert", "fsdp"), None),
            P(("expert", "fsdp"), None),
            P("expert", "fsdp", None),
            P("expert", "fsdp", None),
        ),
        out_specs=P(("expert", "fsdp"), None, None),
        check_vma=False,
    )
```

```python
import jax
import jax.numpy as jnp
from jax import lax
from jax.sharding import PartitionSpec as P


def hidden_block(row_block, gate_rows, up_rows):
    columns = gate_rows.shape[0]
    both = jnp.concatenate([gate_rows, up_rows], axis=0)
    acts = lax.dot_general(
        row_block, both, (((1,), (1,)), ((), ())), preferred_element_type=jnp.float32
    )
    gate_act = acts[:, :columns]
    up_act = acts[:, columns:]
    return (jax.nn.gelu(gate_act, approximate=False) * up_act).astype(jnp.bfloat16)


def local(tokens, expert_ids, router_weight, w_gate, w_up):
    tok_rows, model_width = tokens.shape
    top_count = expert_ids.shape[1]
    experts = lax.axis_size("expert")
    fsdp_size = lax.axis_size("fsdp")
    cap_slots = 5 * tok_rows * top_count // (4 * experts)
    flat_ids = expert_ids.reshape(-1)
    order = jnp.arange(flat_ids.shape[0], dtype=jnp.int32)
    earlier = (order[None, :] < order[:, None]) & (flat_ids[None, :] == flat_ids[:, None])
    slot_rank = jnp.sum(earlier.astype(jnp.int32), axis=1)
    slot_of = flat_ids * cap_slots + slot_rank
    slots = jnp.arange(experts * cap_slots, dtype=jnp.int32)
    placing = (slot_of.reshape(tok_rows, top_count)[:, :, None] == slots).astype(jnp.bfloat16)
    by_token = jnp.sum(placing, axis=1)
    outgoing = lax.dot_general(
        by_token, tokens, (((0,), (0,)), ((), ())), preferred_element_type=jnp.float32
    ).astype(jnp.bfloat16)
    outgoing = outgoing.reshape(experts, cap_slots, model_width)
    gate_rows = w_gate[0]
    up_rows = w_up[0]
    columns = gate_rows.shape[0]
    block = cap_slots * model_width
    dense = outgoing.reshape(experts, block // 128, 128)
    arrived = lax.all_to_all(dense, "expert", split_axis=0, concat_axis=0, tiled=True)
    local_hidden = hidden_block(
        lax.all_gather(arrived.reshape(-1, model_width), "fsdp", axis=0, tiled=True),
        gate_rows,
        up_rows,
    )
    shaped = local_hidden.reshape(fsdp_size, experts, cap_slots, columns)
    wide = -(-columns // 128) * 128
    by_owner = jnp.transpose(shaped, (1, 0, 2, 3))
    by_owner = jnp.pad(by_owner, ((0, 0), (0, 0), (0, 0), (0, wide - columns)))
    by_owner = by_owner.reshape(experts * fsdp_size, cap_slots * wide // 128, 128)
    returned = lax.all_to_all(by_owner, ("expert", "fsdp"), 0, 0, tiled=True)
    returned = returned.reshape(experts, fsdp_size, cap_slots, wide)[..., :columns]
    returned = jnp.transpose(returned, (0, 2, 1, 3)).reshape(experts * cap_slots, -1)
    collected = jnp.take(returned, slot_of.reshape(tok_rows, top_count), axis=0, mode="clip")
    return (router_weight[:, :, None] * collected.astype(jnp.float32)).astype(jnp.bfloat16)


def solution(mesh):
    return jax.shard_map(
        local,
        mesh=mesh,
        in_specs=(
            P(("expert", "fsdp"), None),
            P(("expert", "fsdp"), None),
            P(("expert", "fsdp"), None),
            P("expert", "fsdp", None),
            P("expert", "fsdp", None),
        ),
        out_specs=P(("expert", "fsdp"), None, None),
        check_vma=False,
    )
```

```python
import jax
import jax.numpy as jnp
from jax import lax
from jax.sharding import PartitionSpec as P


def hidden_block(row_block, gate_rows, up_rows):
    columns = gate_rows.shape[0]
    both = jnp.concatenate([gate_rows, up_rows], axis=0)
    acts = lax.dot_general(
        row_block, both, (((1,), (1,)), ((), ())), preferred_element_type=jnp.float32
    )
    gate_act = acts[:, :columns]
    up_act = acts[:, columns:]
    return (jax.nn.gelu(gate_act, approximate=False) * up_act).astype(jnp.bfloat16)


def local(tokens, expert_ids, router_weight, w_gate, w_up):
    tok_rows, model_width = tokens.shape
    top_count = expert_ids.shape[1]
    experts = lax.axis_size("expert")
    fsdp_size = lax.axis_size("fsdp")
    cap_slots = 5 * tok_rows * top_count // (4 * experts)
    flat_ids = expert_ids.reshape(-1)
    order = jnp.arange(flat_ids.shape[0], dtype=jnp.int32)
    earlier = (order[None, :] < order[:, None]) & (flat_ids[None, :] == flat_ids[:, None])
    slot_rank = jnp.sum(earlier.astype(jnp.int32), axis=1)
    slot_of = flat_ids * cap_slots + slot_rank
    slots = jnp.arange(experts * cap_slots, dtype=jnp.int32)
    filled = slot_of[None, :] == slots[:, None]
    owner = jnp.arange(flat_ids.shape[0], dtype=jnp.int32) // top_count
    token_of = jnp.sum(jnp.where(filled, owner[None, :], 0), axis=1)
    outgoing = jnp.take(tokens, token_of, axis=0, mode="clip")
    outgoing = outgoing.reshape(experts, cap_slots, model_width)
    gate_rows = w_gate[0]
    up_rows = w_up[0]
    columns = gate_rows.shape[0]
    block = cap_slots * model_width
    dense = outgoing.reshape(experts, block // 128, 128)
    arrived = lax.all_to_all(dense, "expert", split_axis=0, concat_axis=0, tiled=True)
    local_hidden = hidden_block(
        lax.all_gather(arrived.reshape(-1, model_width), "fsdp", axis=0, tiled=True),
        gate_rows,
        up_rows,
    )
    shaped = local_hidden.reshape(fsdp_size, experts, cap_slots, columns)
    wide = -(-columns // 128) * 128
    by_owner = jnp.transpose(shaped, (1, 0, 2, 3))
    by_owner = jnp.pad(by_owner, ((0, 0), (0, 0), (0, 0), (0, wide - columns)))
    by_owner = by_owner.reshape(experts * fsdp_size, cap_slots * wide // 128, 128)
    returned = lax.all_to_all(by_owner, ("expert", "fsdp"), 0, 0, tiled=True)
    returned = returned.reshape(experts, fsdp_size, cap_slots, wide)[..., :columns]
    returned = jnp.transpose(returned, (0, 2, 1, 3)).reshape(experts * cap_slots, -1)
    collected = jnp.take(returned, slot_of.reshape(tok_rows, top_count), axis=0, mode="clip")
    return (router_weight[:, :, None] * collected.astype(jnp.float32)).astype(jnp.bfloat16)


def solution(mesh):
    return jax.shard_map(
        local,
        mesh=mesh,
        in_specs=(
            P(("expert", "fsdp"), None),
            P(("expert", "fsdp"), None),
            P(("expert", "fsdp"), None),
            P("expert", "fsdp", None),
            P("expert", "fsdp", None),
        ),
        out_specs=P(("expert", "fsdp"), None, None),
        check_vma=False,
    )
```

```python
import jax
import jax.numpy as jnp
from jax import lax
from jax.sharding import PartitionSpec as P


def hidden_block(row_block, gate_rows, up_rows):
    columns = gate_rows.shape[0]
    both = jnp.concatenate([gate_rows, up_rows], axis=0)
    acts = lax.dot_general(
        row_block, both, (((1,), (1,)), ((), ())), preferred_element_type=jnp.float32
    )
    gate_act = acts[:, :columns]
    up_act = acts[:, columns:]
    gelu = gate_act * (1.0 + lax.erf(gate_act * (2.0 ** -0.5))) * 0.5
    return (gelu * up_act).astype(jnp.bfloat16)


def local(tokens, expert_ids, router_weight, w_gate, w_up):
    tok_rows, model_width = tokens.shape
    top_count = expert_ids.shape[1]
    experts = lax.axis_size("expert")
    fsdp_size = lax.axis_size("fsdp")
    cap_slots = 5 * tok_rows * top_count // (4 * experts)
    flat_ids = expert_ids.reshape(-1)
    order = jnp.arange(flat_ids.shape[0], dtype=jnp.int32)
    earlier = (order[None, :] < order[:, None]) & (flat_ids[None, :] == flat_ids[:, None])
    slot_rank = jnp.sum(earlier.astype(jnp.int32), axis=1)
    slot_of = flat_ids * cap_slots + slot_rank
    slots = jnp.arange(experts * cap_slots, dtype=jnp.int32)
    placing = (slot_of.reshape(tok_rows, top_count)[:, :, None] == slots).astype(jnp.bfloat16)
    by_token = jnp.sum(placing, axis=1)
    outgoing = lax.dot_general(
        by_token, tokens, (((0,), (0,)), ((), ())), preferred_element_type=jnp.float32
    ).astype(jnp.bfloat16)
    outgoing = outgoing.reshape(experts, cap_slots, model_width)
    gate_rows = w_gate[0]
    up_rows = w_up[0]
    columns = gate_rows.shape[0]
    block = cap_slots * model_width
    dense = outgoing.reshape(experts, block // 128, 128)
    arrived = lax.all_to_all(dense, "expert", split_axis=0, concat_axis=0, tiled=True)
    local_hidden = hidden_block(
        lax.all_gather(arrived.reshape(-1, model_width), "fsdp", axis=0, tiled=True),
        gate_rows,
        up_rows,
    )
    shaped = local_hidden.reshape(fsdp_size, experts, cap_slots, columns)
    wide = -(-columns // 128) * 128
    by_owner = jnp.transpose(shaped, (1, 0, 2, 3))
    by_owner = jnp.pad(by_owner, ((0, 0), (0, 0), (0, 0), (0, wide - columns)))
    by_owner = by_owner.reshape(experts * fsdp_size, cap_slots * wide // 128, 128)
    returned = lax.all_to_all(by_owner, ("expert", "fsdp"), 0, 0, tiled=True)
    returned = returned.reshape(experts, fsdp_size, cap_slots, wide)[..., :columns]
    returned = jnp.transpose(returned, (0, 2, 1, 3)).reshape(experts * cap_slots, -1)
    collected = jnp.take(returned, slot_of.reshape(tok_rows, top_count), axis=0, mode="clip")
    return (router_weight[:, :, None] * collected.astype(jnp.float32)).astype(jnp.bfloat16)


def solution(mesh):
    return jax.shard_map(
        local,
        mesh=mesh,
        in_specs=(
            P(("expert", "fsdp"), None),
            P(("expert", "fsdp"), None),
            P(("expert", "fsdp"), None),
            P("expert", "fsdp", None),
            P("expert", "fsdp", None),
        ),
        out_specs=P(("expert", "fsdp"), None, None),
        check_vma=False,
    )
```

```python
import jax
import jax.numpy as jnp
from jax import lax
from jax.sharding import PartitionSpec as P


def hidden_block(row_block, gate_rows, up_rows):
    columns, width = gate_rows.shape
    wide = -(-columns // 128) * 128
    pad = jnp.zeros((wide - columns, width), gate_rows.dtype)
    both = jnp.concatenate([gate_rows, pad, up_rows, pad], axis=0)
    acts = lax.dot_general(
        row_block, both, (((1,), (1,)), ((), ())), preferred_element_type=jnp.float32
    )
    gate_act = acts[:, :wide]
    up_act = acts[:, wide:]
    gelu = gate_act * (1.0 + lax.erf(gate_act * (2.0 ** -0.5))) * 0.5
    return (gelu * up_act).astype(jnp.bfloat16)


def local(tokens, expert_ids, router_weight, w_gate, w_up):
    tok_rows, model_width = tokens.shape
    top_count = expert_ids.shape[1]
    experts = lax.axis_size("expert")
    fsdp_size = lax.axis_size("fsdp")
    cap_slots = 5 * tok_rows * top_count // (4 * experts)
    flat_ids = expert_ids.reshape(-1)
    order = jnp.arange(flat_ids.shape[0], dtype=jnp.int32)
    earlier = (order[None, :] < order[:, None]) & (flat_ids[None, :] == flat_ids[:, None])
    slot_rank = jnp.sum(earlier.astype(jnp.int32), axis=1)
    slot_of = flat_ids * cap_slots + slot_rank
    slots = jnp.arange(experts * cap_slots, dtype=jnp.int32)
    placing = (slot_of.reshape(tok_rows, top_count)[:, :, None] == slots).astype(jnp.bfloat16)
    by_token = jnp.sum(placing, axis=1)
    outgoing = lax.dot_general(
        by_token, tokens, (((0,), (0,)), ((), ())), preferred_element_type=jnp.float32
    ).astype(jnp.bfloat16)
    outgoing = outgoing.reshape(experts, cap_slots, model_width)
    gate_rows = w_gate[0]
    up_rows = w_up[0]
    columns = gate_rows.shape[0]
    block = cap_slots * model_width
    dense = outgoing.reshape(experts, block // 128, 128)
    arrived = lax.all_to_all(dense, "expert", split_axis=0, concat_axis=0, tiled=True)
    local_hidden = hidden_block(
        lax.all_gather(arrived.reshape(-1, model_width), "fsdp", axis=0, tiled=True),
        gate_rows,
        up_rows,
    )
    wide = local_hidden.shape[1]
    shaped = local_hidden.reshape(fsdp_size, experts, cap_slots, wide)
    by_owner = jnp.transpose(shaped, (1, 0, 2, 3))
    by_owner = by_owner.reshape(experts * fsdp_size, cap_slots * wide // 128, 128)
    returned = lax.all_to_all(by_owner, ("expert", "fsdp"), 0, 0, tiled=True)
    returned = returned.reshape(experts, fsdp_size, cap_slots, wide)[..., :columns]
    returned = jnp.transpose(returned, (0, 2, 1, 3)).reshape(experts * cap_slots, -1)
    collected = jnp.take(returned, slot_of.reshape(tok_rows, top_count), axis=0, mode="clip")
    return (router_weight[:, :, None] * collected.astype(jnp.float32)).astype(jnp.bfloat16)


def solution(mesh):
    return jax.shard_map(
        local,
        mesh=mesh,
        in_specs=(
            P(("expert", "fsdp"), None),
            P(("expert", "fsdp"), None),
            P(("expert", "fsdp"), None),
            P("expert", "fsdp", None),
            P("expert", "fsdp", None),
        ),
        out_specs=P(("expert", "fsdp"), None, None),
        check_vma=False,
    )
```

```python
import jax
import jax.numpy as jnp
from jax import lax
from jax.sharding import PartitionSpec as P


def hidden_block(row_block, gate_rows, up_rows):
    columns = gate_rows.shape[0]
    both = jnp.concatenate([gate_rows, up_rows], axis=0)
    acts = lax.dot_general(
        row_block, both, (((1,), (1,)), ((), ())), preferred_element_type=jnp.float32
    )
    gate_act = acts[:, :columns]
    up_act = acts[:, columns:]
    gelu = gate_act * (1.0 + lax.erf(gate_act * (2.0 ** -0.5))) * 0.5
    return (gelu * up_act).astype(jnp.bfloat16)


def local(tokens, expert_ids, router_weight, w_gate, w_up):
    tok_rows, model_width = tokens.shape
    top_count = expert_ids.shape[1]
    experts = lax.axis_size("expert")
    fsdp_size = lax.axis_size("fsdp")
    cap_slots = 5 * tok_rows * top_count // (4 * experts)
    flat_ids = expert_ids.T.reshape(-1)
    order = jnp.arange(flat_ids.shape[0], dtype=jnp.int32)
    earlier = (order[None, :] < order[:, None]) & (flat_ids[None, :] == flat_ids[:, None])
    slot_rank = jnp.sum(earlier.astype(jnp.int32), axis=1)
    slot_of = (flat_ids * cap_slots + slot_rank).reshape(top_count, tok_rows).T.reshape(-1)
    slots = jnp.arange(experts * cap_slots, dtype=jnp.int32)
    placing = (slot_of.reshape(tok_rows, top_count)[:, :, None] == slots).astype(jnp.bfloat16)
    by_token = jnp.sum(placing, axis=1)
    outgoing = lax.dot_general(
        by_token, tokens, (((0,), (0,)), ((), ())), preferred_element_type=jnp.float32
    ).astype(jnp.bfloat16)
    outgoing = outgoing.reshape(experts, cap_slots, model_width)
    gate_rows = w_gate[0]
    up_rows = w_up[0]
    columns = gate_rows.shape[0]
    block = cap_slots * model_width
    dense = outgoing.reshape(experts, block // 128, 128)
    arrived = lax.all_to_all(dense, "expert", split_axis=0, concat_axis=0, tiled=True)
    local_hidden = hidden_block(
        lax.all_gather(arrived.reshape(-1, model_width), "fsdp", axis=0, tiled=True),
        gate_rows,
        up_rows,
    )
    shaped = local_hidden.reshape(fsdp_size, experts, cap_slots, columns)
    wide = -(-columns // 128) * 128
    by_owner = jnp.transpose(shaped, (1, 0, 2, 3))
    by_owner = jnp.pad(by_owner, ((0, 0), (0, 0), (0, 0), (0, wide - columns)))
    by_owner = by_owner.reshape(experts * fsdp_size, cap_slots * wide // 128, 128)
    returned = lax.all_to_all(by_owner, ("expert", "fsdp"), 0, 0, tiled=True)
    returned = returned.reshape(experts, fsdp_size, cap_slots, wide)[..., :columns]
    returned = jnp.transpose(returned, (0, 2, 1, 3)).reshape(experts * cap_slots, -1)
    collected = jnp.take(returned, slot_of.reshape(tok_rows, top_count), axis=0, mode="clip")
    return (router_weight[:, :, None] * collected.astype(jnp.float32)).astype(jnp.bfloat16)


def solution(mesh):
    return jax.shard_map(
        local,
        mesh=mesh,
        in_specs=(
            P(("expert", "fsdp"), None),
            P(("expert", "fsdp"), None),
            P(("expert", "fsdp"), None),
            P("expert", "fsdp", None),
            P("expert", "fsdp", None),
        ),
        out_specs=P(("expert", "fsdp"), None, None),
        check_vma=False,
    )
```
